128 devices in a mesh: leaf: 16 (over z, x), panel: 8 (over y, core).
Axes of the slice: x: 4, y: 4, z: 4, core: 2. Of those that a mesh axis runs over, the one named last changes fastest.
Arguments:
- child_front: float32 [16, 2048, 2048], P('leaf', 'panel'), as said below
- child_panel: bfloat16 [16, 2048, 4096], P('leaf'), may hold values from -0.03125 to 0.03125
- parent_front: float32 [4096, 4096], P('leaf', 'panel'), as said below
- tile_map: int32 [16, 8], P('leaf'), may hold values from 0 to 15, as said below
- tile_count: int32 [16], P('leaf'), may hold values from 2 to 8, as said below
Outputs:
- eliminated: float32 [4096, 4096], P('leaf', 'panel')
The draws below stay inside these ranges and needn't reach their ends.
Inputs may be any that keep to these rules, and one draw needn't show every extreme that they name: `tile_count`: some child has 8 live tiles and some child has 2. `tile_map`: for child c the first tile_count[c] entries are distinct and rising; the other entries are 0. Each child's block is symmetric, and child_front[c] - child_panel[c] child_panel[c]^T is positive definite. `parent_front`: symmetric positive definite.
All inputs are finite; a program needn't handle non-finite values.
Results may differ from the reference program's by a relative error of at most 0.0003.
Values sent between devices are 32-bit elements; how exact they have to be, the bound alone decides.
No kernel may reach another device: no remote copies, remote signals or barrier semaphores. Data moves between devices by JAX's collectives and lax.ppermute only.
A program may use at most 128 MiB of HBM per device.

```python
import math
import jax
import jax.numpy as jnp
from jax import lax

TILE = 256
NF = 4096
CB = 2048
PC = 4096
STEPS = 4
CT = 8
FT = 16
CHILDREN = 16


kernel_reach = 0.1


def screened_matrix(key, lead, order, amplitude, lowest, highest, place_top, scale_low, scale_high):
    key_place, key_scale, key_diag = jax.random.split(key, 3)
    shape = lead + (order,)
    places = jax.random.uniform(key_place, shape, jnp.float32, 0.0, place_top)
    scales = jnp.exp(jax.random.uniform(key_scale, shape, jnp.float32, math.log(scale_low), math.log(scale_high)))
    diag_values = jnp.exp(jax.random.uniform(key_diag, shape, jnp.float32, math.log(lowest), math.log(highest)))
    distance = jnp.abs(places[..., :, None] - places[..., None, :])
    coupling = amplitude * scales[..., :, None] * scales[..., None, :] * jnp.exp(-distance / kernel_reach)
    on_diagonal = jnp.arange(order)[:, None] == jnp.arange(order)[None, :]
    return jnp.where(on_diagonal, coupling + diag_values[..., :, None], coupling)


def draw_child_front(key, part):
    base = jax.random.fold_in(key, 3)
    return screened_matrix(base, (CHILDREN,), CB, 2.0, 1.2, 2.4, 1.0, 0.75, 1.33)


def draw_parent_front(key, part):
    base = jax.random.fold_in(key, 5)
    return screened_matrix(base, (), NF, 2.0, 1.0, 2.0, 1.0, 0.75, 1.33)


def tile_layout(key):
    base = jax.random.fold_in(key, 41)
    key_count, key_pick, key_order = jax.random.split(base, 3)
    counts = jax.random.randint(key_count, (CHILDREN,), 2, CT + 1)
    picked = jax.random.permutation(key_pick, CHILDREN)
    counts = counts.at[picked[0]].set(CT).at[picked[1]].set(2)
    scores = jax.random.randint(key_order, (CHILDREN, FT), 0, 2 ** 20) * FT + jnp.arange(FT)[None, :]
    shuffled = jnp.argsort(scores, axis=1, stable=True)[:, :CT]
    position = jnp.arange(CT)[None, :]
    live_tiles = position < counts[:, None]
    scored = jnp.where(live_tiles, shuffled, FT + position)
    ordered = jnp.sort(scored, axis=1)
    maps = jnp.where(live_tiles, ordered, 0)
    return (maps.astype(jnp.int32), counts.astype(jnp.int32))


def draw_tile_map(key, part):
    return tile_layout(key)[0]


def draw_tile_count(key, part):
    return tile_layout(key)[1]


def block_scale(key, dims, cuts, least, high):
    gain, own = 1.0, jax.random.fold_in(key, 6)
    for dim, parts in cuts:
        steps = jnp.exp(jax.random.uniform(jax.random.fold_in(own, dim), (parts,), jnp.float32, least / len(cuts), high / len(cuts)))
        gain = gain * jnp.repeat(steps, dims[dim] // parts).reshape([-1 if axis == dim else 1 for axis in range(len(dims))])
    return gain


def noise(stream_key, shape, deviation, bound, cuts=(), kind=jnp.bfloat16):
    drawn = deviation * jax.random.normal(stream_key, shape, jnp.float32)
    if cuts:
        drawn = drawn * block_scale(stream_key, shape, cuts, -0.22, 0.18)
    return jnp.clip(drawn, -bound, bound).astype(kind)


def setup_inputs(seed: int = 0) -> dict:
    streams_of = jax.random.split(jax.random.key(seed), 6)
    return {
        "child_front": draw_child_front(jax.random.fold_in(streams_of[5], 71), 0),
        "child_panel": noise(streams_of[1], (CHILDREN, CB, PC), (8 * PC) ** -0.5, 0.03125, ((0, 16),)),
        "parent_front": draw_parent_front(jax.random.fold_in(streams_of[5], 71), 0),
        "tile_map": draw_tile_map(jax.random.fold_in(streams_of[5], 71), 0),
        "tile_count": draw_tile_count(jax.random.fold_in(streams_of[5], 71), 0),
    }


def reference(child_front, child_panel, parent_front, tile_map, tile_count):
    highest = lax.Precision.HIGHEST
    pivot_span = STEPS * TILE
    targets = jnp.arange(FT, dtype=jnp.int32)
    front_block = parent_front
    for child_index in range(CHILDREN):
        panel_rows = child_panel[child_index]
        update = child_front[child_index] - lax.dot_general(panel_rows.astype(jnp.float32), panel_rows.astype(jnp.float32), (((1,), (1,)), ((), ())), preferred_element_type=jnp.float32)
        live_tiles = jnp.arange(CT, dtype=jnp.int32) < tile_count[child_index]
        chosen = ((tile_map[child_index][None, :] == targets[:, None]) & live_tiles[None, :]).astype(jnp.float32)
        blocks = update.reshape(CT, TILE, CT, TILE)
        placed = jnp.einsum('ft,taub->faub', chosen, blocks, precision=highest)
        placed = jnp.einsum('faub,gu->fagb', placed, chosen, precision=highest)
        front_block = front_block + placed.reshape(NF, NF)
    factor = jnp.linalg.cholesky(front_block[:pivot_span, :pivot_span])
    below = lax.linalg.triangular_solve(factor, front_block[pivot_span:, :pivot_span], left_side=False, lower=True, transpose_a=True)
    rest = front_block[pivot_span:, pivot_span:] - jnp.dot(below.astype(jnp.float32), below.T.astype(jnp.float32), precision=highest, preferred_element_type=jnp.float32)
    upper_rows = jnp.concatenate([factor, jnp.zeros((pivot_span, NF - pivot_span), jnp.float32)], axis=1)
    lower_rows = jnp.concatenate([below, rest], axis=1)
    return jnp.concatenate([upper_rows, lower_rows], axis=0)
```

```python
import jax
import jax.numpy as jnp
from jax import lax
from jax.sharding import PartitionSpec as P

TILE = 256
NF = 4096
CB = 2048
STEPS = 4


def shards(child_front, child_panel, parent_front, tile_map, tile_count):
    highest = lax.Precision.HIGHEST
    panel_count = lax.axis_size("panel")
    leaf_count = lax.axis_size("leaf")
    leaf_id = lax.axis_index("leaf")
    panel_id = lax.axis_index("panel")
    tiles_child = CB // TILE
    tiles_front = NF // TILE
    pivot_span = STEPS * TILE
    child_rows = child_front.shape[1]
    height = parent_front.shape[0]
    col_width = parent_front.shape[1]
    slab = pivot_span // panel_count
    slabs_per_block = col_width // slab

    panel_all = child_panel[0]
    own_panel = lax.dynamic_slice_in_dim(panel_all, panel_id * child_rows, child_rows, 0)
    update = child_front[0] - lax.dot_general(
        own_panel, panel_all, (((1,), (1,)), ((), ())), preferred_element_type=jnp.float32
    )
    mapped = tile_map[0]
    live_tiles = jnp.arange(tiles_child, dtype=jnp.int32) < tile_count[0]
    everywhere = jnp.arange(tiles_front, dtype=jnp.int32)
    chosen = ((mapped[None, :] == everywhere[:, None]) & live_tiles[None, :]).astype(jnp.float32)
    placed = jnp.einsum(
        "rtb,ft->rfb", update.reshape(child_rows, tiles_child, TILE), chosen, precision=highest
    ).reshape(child_rows, NF)
    regular = placed.reshape(child_rows, panel_count, col_width).transpose(1, 0, 2)
    pivot_slabs = placed[:, :pivot_span].reshape(child_rows, panel_count, slab).transpose(1, 0, 2)
    parent_slabs = parent_front.reshape(height, slabs_per_block, slab).transpose(1, 0, 2)
    parent_slabs = jnp.tile(parent_slabs, (panel_count // slabs_per_block, 1, 1))
    dest = jnp.arange(panel_count, dtype=jnp.int32)
    parent_slabs = jnp.where(
        (dest // slabs_per_block == panel_id)[:, None, None], parent_slabs, 0.0
    )
    send = jnp.concatenate([regular, pivot_slabs, parent_slabs], axis=2)
    moved = lax.all_to_all(send, "panel", split_axis=0, concat_axis=0, tiled=True)
    child_part = moved[:, :, : col_width + slab]
    parent_slab = jnp.sum(moved[:, :, col_width + slab :], axis=0)
    targets = jnp.arange(leaf_count * height // TILE, dtype=jnp.int32)
    picked = ((mapped[None, :] == targets[:, None]) & live_tiles[None, :]).astype(jnp.float32)
    summed = jnp.einsum("ft,tbc->fbc", picked, child_part, precision=highest)
    own_parent = jnp.concatenate([parent_front, parent_slab], axis=1)
    summed = summed.at[leaf_id].add(own_parent)
    reduced = lax.psum_scatter(
        summed.reshape(leaf_count * height, col_width + slab),
        "leaf",
        scatter_dimension=0,
        tiled=True,
    )
    front_block = reduced[:, :col_width]
    my_slab = reduced[:, col_width:]

    gathered = lax.all_gather(my_slab, ("leaf", "panel"), axis=0, tiled=False)
    gathered = gathered.reshape(leaf_count, panel_count, height, slab)

    def rows_of(tiles):
        count = tiles.shape[0]
        return tiles.transpose(0, 2, 1, 3).reshape(count * height, panel_count * slab)

    top_tiles = pivot_span // height
    pivot_block = rows_of(gathered[:top_tiles])
    own_rows = rows_of(lax.dynamic_slice_in_dim(gathered, leaf_id, 1, 0))
    col_tiles = col_width // height
    col_rows = rows_of(lax.dynamic_slice_in_dim(gathered, panel_id * col_tiles, col_tiles, 0))

    factor = jnp.linalg.cholesky(pivot_block)
    solved = lax.linalg.triangular_solve(
        factor,
        jnp.concatenate([own_rows, col_rows], axis=0),
        left_side=False,
        lower=True,
        transpose_a=True,
    )
    factor_rows = lax.dynamic_slice_in_dim(
        factor, jnp.minimum(leaf_id, top_tiles - 1) * height, height, 0
    )
    row_part = jnp.where(leaf_id < top_tiles, factor_rows, solved[:height])
    col_part = solved[height:]
    rest = front_block - lax.dot_general(
        row_part,
        col_part,
        (((1,), (1,)), ((), ())),
        precision=highest,
        preferred_element_type=jnp.float32,
    )
    pivot_blocks = pivot_span // col_width
    pivot_out = lax.dynamic_slice_in_dim(
        row_part, jnp.minimum(panel_id, pivot_blocks - 1) * col_width, col_width, 1
    )
    upper = jnp.where(leaf_id < top_tiles, 0.0, rest)
    return jnp.where(panel_id < pivot_blocks, pivot_out, upper)


def solution(mesh):
    placed = (
        P("leaf", "panel", None),
        P("leaf", None, None),
        P("leaf", "panel"),
        P("leaf", None),
        P("leaf"),
    )
    return jax.shard_map(
        shards, mesh=mesh, in_specs=placed, out_specs=P("leaf", "panel"), check_vma=False
    )
```

```python
import jax
import jax.numpy as jnp
from jax import lax
from jax.sharding import PartitionSpec as P

TILE = 256
NF = 4096
CB = 2048
STEPS = 4


def shards(child_front, child_panel, parent_front, tile_map, tile_count):
    highest = lax.Precision.HIGHEST
    panel_count = lax.axis_size("panel")
    leaf_count = lax.axis_size("leaf")
    leaf_id = lax.axis_index("leaf")
    panel_id = lax.axis_index("panel")
    tiles_child = CB // TILE
    tiles_front = NF // TILE
    pivot_span = STEPS * TILE
    child_rows = child_front.shape[1]
    height = parent_front.shape[0]
    col_width = parent_front.shape[1]
    slab = pivot_span // panel_count
    slabs_per_block = col_width // slab

    panel_all = child_panel[0]
    own_panel = lax.dynamic_slice_in_dim(panel_all, panel_id * child_rows, child_rows, 0)
    update = child_front[0] - lax.dot_general(
        own_panel, panel_all, (((1,), (1,)), ((), ())), preferred_element_type=jnp.float32
    )
    mapped = tile_map[0]
    live_tiles = jnp.arange(tiles_child, dtype=jnp.int32) < tile_count[0]
    everywhere = jnp.arange(tiles_front, dtype=jnp.int32)
    chosen = ((mapped[None, :] == everywhere[:, None]) & live_tiles[None, :]).astype(jnp.float32)
    placed = jnp.einsum(
        "rtb,ft->rfb", update.reshape(child_rows, tiles_child, TILE), chosen, precision=highest
    ).reshape(child_rows, NF)
    regular = placed.reshape(child_rows, panel_count, col_width).transpose(1, 0, 2)
    pivot_slabs = placed[:, :pivot_span].reshape(child_rows, panel_count, slab).transpose(1, 0, 2)
    parent_slabs = parent_front.reshape(height, slabs_per_block, slab).transpose(1, 0, 2)
    parent_slabs = jnp.tile(parent_slabs, (panel_count // slabs_per_block, 1, 1))
    dest = jnp.arange(panel_count, dtype=jnp.int32)
    parent_slabs = jnp.where(
        (dest // slabs_per_block == panel_id)[:, None, None], parent_slabs, 0.0
    )
    send = jnp.concatenate([regular, pivot_slabs, parent_slabs], axis=2)
    moved = lax.all_to_all(send, "panel", split_axis=0, concat_axis=0, tiled=True)
    child_part = moved[:, :, : col_width + slab]
    parent_slab = jnp.sum(moved[:, :, col_width + slab :], axis=0)
    targets = jnp.arange(leaf_count * height // TILE, dtype=jnp.int32)
    picked = ((mapped[None, :] == targets[:, None]) & live_tiles[None, :]).astype(jnp.float32)
    summed = jnp.einsum("ft,tbc->fbc", picked, child_part, precision=highest)
    own_parent = jnp.concatenate([parent_front, parent_slab], axis=1)
    summed = summed.at[leaf_id].add(own_parent)
    summed = summed.reshape(leaf_count * height, col_width + slab)
    top_share = pivot_span // leaf_count
    slab_rows = summed[:, col_width:]
    slab_rows = jnp.concatenate(
        [
            slab_rows[:pivot_span].reshape(leaf_count, top_share, slab),
            slab_rows[pivot_span:].reshape(leaf_count, height - top_share, slab),
        ],
        axis=1,
    ).reshape(leaf_count * height, slab)
    summed = jnp.concatenate([summed[:, :col_width], slab_rows], axis=1)
    reduced = lax.psum_scatter(summed, "leaf", scatter_dimension=0, tiled=True)
    front_block = reduced[:, :col_width]
    my_slab = reduced[:, col_width:]

    def assemble(piece):
        rows = piece.shape[0]
        got = lax.all_gather(piece, ("leaf", "panel"), axis=0, tiled=False)
        got = got.reshape(leaf_count, panel_count, rows, slab).transpose(0, 2, 1, 3)
        return got.reshape(leaf_count * rows, panel_count * slab)

    pivot_block = assemble(my_slab[:top_share])
    lower_block = assemble(my_slab[top_share:])

    blocks = pivot_span // TILE
    eye = jnp.eye(TILE, dtype=jnp.float32)
    work = pivot_block
    factor_cols = []
    inverses = []
    for k in range(blocks):
        lo, hi = k * TILE, (k + 1) * TILE
        diag = lax.linalg.cholesky(work[lo:hi, lo:hi], symmetrize_input=True)
        diag = jnp.tril(diag)
        inverse = lax.linalg.triangular_solve(diag, eye, left_side=True, lower=True)
        inverses.append(inverse)
        if k + 1 < blocks:
            below = jnp.dot(work[hi:, lo:hi], inverse.T, precision=highest)
            work = work.at[hi:, hi:].add(-jnp.dot(below, below.T, precision=highest))
            column = jnp.concatenate([jnp.zeros((lo, TILE), jnp.float32), diag, below], axis=0)
        else:
            column = jnp.concatenate([jnp.zeros((lo, TILE), jnp.float32), diag], axis=0)
        factor_cols.append(column)
    factor = jnp.concatenate(factor_cols, axis=1)

    top_tiles = pivot_span // height
    own_rows = lax.dynamic_slice_in_dim(
        lower_block, jnp.maximum(leaf_id - top_tiles, 0) * height, height, 0
    )
    col_rows = lax.dynamic_slice_in_dim(
        lower_block,
        jnp.maximum(panel_id - pivot_span // col_width, 0) * col_width,
        col_width,
        0,
    )
    extra = jnp.concatenate([own_rows, col_rows], axis=0)
    solved = []
    for k in range(blocks):
        lo, hi = k * TILE, (k + 1) * TILE
        part = extra[:, lo:hi]
        if k:
            part = part - jnp.dot(
                jnp.concatenate(solved, axis=1), factor[lo:hi, :lo].T, precision=highest
            )
        solved.append(jnp.dot(part, inverses[k].T, precision=highest))
    solved = jnp.concatenate(solved, axis=1)

    factor_rows = lax.dynamic_slice_in_dim(
        factor, jnp.minimum(leaf_id, top_tiles - 1) * height, height, 0
    )
    row_part = jnp.where(leaf_id < top_tiles, factor_rows, solved[:height])
    col_part = solved[height:]
    rest = front_block - lax.dot_general(
        row_part,
        col_part,
        (((1,), (1,)), ((), ())),
        precision=highest,
        preferred_element_type=jnp.float32,
    )
    pivot_blocks = pivot_span // col_width
    pivot_out = lax.dynamic_slice_in_dim(
        row_part, jnp.minimum(panel_id, pivot_blocks - 1) * col_width, col_width, 1
    )
    upper = jnp.where(leaf_id < top_tiles, 0.0, rest)
    return jnp.where(panel_id < pivot_blocks, pivot_out, upper)


def solution(mesh):
    placed = (
        P("leaf", "panel", None),
        P("leaf", None, None),
        P("leaf", "panel"),
        P("leaf", None),
        P("leaf"),
    )
    return jax.shard_map(
        shards, mesh=mesh, in_specs=placed, out_specs=P("leaf", "panel"), check_vma=False
    )
```

```python
import jax
import jax.numpy as jnp
from jax import lax
from jax.sharding import PartitionSpec as P

TILE = 256
NF = 4096
CB = 2048
STEPS = 4
FACTOR_TILE = 128


def shards(child_front, child_panel, parent_front, tile_map, tile_count):
    highest = lax.Precision.HIGHEST
    panel_count = lax.axis_size("panel")
    leaf_count = lax.axis_size("leaf")
    leaf_id = lax.axis_index("leaf")
    panel_id = lax.axis_index("panel")
    tiles_child = CB // TILE
    tiles_front = NF // TILE
    pivot_span = STEPS * TILE
    child_rows = child_front.shape[1]
    height = parent_front.shape[0]
    col_width = parent_front.shape[1]
    slab = pivot_span // panel_count
    slabs_per_block = col_width // slab

    panel_all = child_panel[0]
    own_panel = lax.dynamic_slice_in_dim(panel_all, panel_id * child_rows, child_rows, 0)
    update = child_front[0] - lax.dot_general(
        own_panel, panel_all, (((1,), (1,)), ((), ())), preferred_element_type=jnp.float32
    )
    mapped = tile_map[0]
    live_tiles = jnp.arange(tiles_child, dtype=jnp.int32) < tile_count[0]
    everywhere = jnp.arange(tiles_front, dtype=jnp.int32)
    chosen = ((mapped[None, :] == everywhere[:, None]) & live_tiles[None, :]).astype(jnp.float32)
    placed = jnp.einsum(
        "rtb,ft->rfb", update.reshape(child_rows, tiles_child, TILE), chosen, precision=highest
    ).reshape(child_rows, NF)
    regular = placed.reshape(child_rows, panel_count, col_width).transpose(1, 0, 2)
    pivot_slabs = placed[:, :pivot_span].reshape(child_rows, panel_count, slab).transpose(1, 0, 2)
    parent_slabs = parent_front.reshape(height, slabs_per_block, slab).transpose(1, 0, 2)
    parent_slabs = jnp.tile(parent_slabs, (panel_count // slabs_per_block, 1, 1))
    dest = jnp.arange(panel_count, dtype=jnp.int32)
    parent_slabs = jnp.where(
        (dest // slabs_per_block == panel_id)[:, None, None], parent_slabs, 0.0
    )
    send = jnp.concatenate([regular, pivot_slabs, parent_slabs], axis=2)
    moved = lax.all_to_all(send, "panel", split_axis=0, concat_axis=0, tiled=True)
    child_part = moved[:, :, : col_width + slab]
    parent_slab = jnp.sum(moved[:, :, col_width + slab :], axis=0)
    targets = jnp.arange(leaf_count * height // TILE, dtype=jnp.int32)
    picked = ((mapped[None, :] == targets[:, None]) & live_tiles[None, :]).astype(jnp.float32)
    own_parent = jnp.concatenate([parent_front, parent_slab], axis=1)
    picked = jnp.concatenate([picked, (targets == leaf_id).astype(jnp.float32)[:, None]], axis=1)
    sources = jnp.concatenate([child_part, own_parent[None]], axis=0)
    summed = jnp.einsum("ft,tbc->fbc", picked, sources, precision=highest)
    summed = summed.reshape(leaf_count * height, col_width + slab)
    top_share = pivot_span // leaf_count
    slab_rows = summed[:, col_width:]
    slab_rows = jnp.concatenate(
        [
            slab_rows[:pivot_span].reshape(leaf_count, top_share, slab),
            slab_rows[pivot_span:].reshape(leaf_count, height - top_share, slab),
        ],
        axis=1,
    ).reshape(leaf_count * height, slab)
    summed = jnp.concatenate([summed[:, :col_width], slab_rows], axis=1)
    reduced = lax.psum_scatter(summed, "leaf", scatter_dimension=0, tiled=True)
    front_block = reduced[:, :col_width]
    my_slab = reduced[:, col_width:]

    def assemble(piece):
        rows = piece.shape[0]
        got = lax.all_gather(piece, ("leaf", "panel"), axis=0, tiled=False)
        got = got.reshape(leaf_count, panel_count, rows, slab).transpose(0, 2, 1, 3)
        return got.reshape(leaf_count * rows, panel_count * slab)

    pivot_block = assemble(my_slab[:top_share])
    lower_share = height - top_share
    lower_pieces = lax.all_gather(my_slab[top_share:], ("leaf", "panel"), axis=0, tiled=False)
    lower_pieces = lower_pieces.reshape(leaf_count, panel_count, lower_share, slab)

    def lower_rows(first, count):
        span = -(-(count + lower_share - 1) // lower_share)
        start = jnp.minimum(first // lower_share, leaf_count - span)
        pieces = lax.dynamic_slice_in_dim(lower_pieces, start, span, 0)
        pieces = pieces.transpose(0, 2, 1, 3).reshape(span * lower_share, panel_count * slab)
        return lax.dynamic_slice_in_dim(pieces, first - start * lower_share, count, 0)

    blocks = pivot_span // FACTOR_TILE
    eye = jnp.eye(FACTOR_TILE, dtype=jnp.float32)
    work = pivot_block
    factor_cols = []
    inverses = []
    for k in range(blocks):
        lo, hi = k * FACTOR_TILE, (k + 1) * FACTOR_TILE
        diag = lax.linalg.cholesky(work[lo:hi, lo:hi], symmetrize_input=True)
        diag = jnp.tril(diag)
        inverse = lax.linalg.triangular_solve(diag, eye, left_side=True, lower=True)
        inverses.append(inverse)
        if k + 1 < blocks:
            below = jnp.dot(work[hi:, lo:hi], inverse.T, precision=highest)
            work = work.at[hi:, hi:].add(-jnp.dot(below, below.T, precision=highest))
            column = jnp.concatenate([jnp.zeros((lo, FACTOR_TILE), jnp.float32), diag, below], axis=0)
        else:
            column = jnp.concatenate([jnp.zeros((lo, FACTOR_TILE), jnp.float32), diag], axis=0)
        factor_cols.append(column)
    factor = jnp.concatenate(factor_cols, axis=1)

    top_tiles = pivot_span // height
    own_rows = lower_rows(jnp.maximum(leaf_id - top_tiles, 0) * height, height)
    col_rows = lower_rows(jnp.maximum(panel_id - pivot_span // col_width, 0) * col_width, col_width)
    extra = jnp.concatenate([own_rows, col_rows], axis=0)
    solved = []
    for k in range(blocks):
        lo, hi = k * FACTOR_TILE, (k + 1) * FACTOR_TILE
        part = extra[:, lo:hi]
        if k:
            part = part - jnp.dot(
                jnp.concatenate(solved, axis=1), factor[lo:hi, :lo].T, precision=highest
            )
        solved.append(jnp.dot(part, inverses[k].T, precision=highest))
    solved = jnp.concatenate(solved, axis=1)

    factor_rows = lax.dynamic_slice_in_dim(
        factor, jnp.minimum(leaf_id, top_tiles - 1) * height, height, 0
    )
    row_part = jnp.where(leaf_id < top_tiles, factor_rows, solved[:height])
    col_part = solved[height:]
    rest = front_block - lax.dot_general(
        row_part,
        col_part,
        (((1,), (1,)), ((), ())),
        precision=highest,
        preferred_element_type=jnp.float32,
    )
    pivot_blocks = pivot_span // col_width
    pivot_out = lax.dynamic_slice_in_dim(
        row_part, jnp.minimum(panel_id, pivot_blocks - 1) * col_width, col_width, 1
    )
    upper = jnp.where(leaf_id < top_tiles, 0.0, rest)
    return jnp.where(panel_id < pivot_blocks, pivot_out, upper)


def solution(mesh):
    placed = (
        P("leaf", "panel", None),
        P("leaf", None, None),
        P("leaf", "panel"),
        P("leaf", None),
        P("leaf"),
    )
    return jax.shard_map(
        shards, mesh=mesh, in_specs=placed, out_specs=P("leaf", "panel"), check_vma=False
    )
```

```python
import jax
import jax.numpy as jnp
from jax import lax
from jax.sharding import PartitionSpec as P

TILE = 256
NF = 4096
CB = 2048
STEPS = 4
FACTOR_TILE = 128


def shards(child_front, child_panel, parent_front, tile_map, tile_count):
    highest = lax.Precision.HIGHEST
    panel_count = lax.axis_size("panel")
    leaf_count = lax.axis_size("leaf")
    leaf_id = lax.axis_index("leaf")
    panel_id = lax.axis_index("panel")
    tiles_child = CB // TILE
    tiles_front = NF // TILE
    pivot_span = STEPS * TILE
    child_rows = child_front.shape[1]
    height = parent_front.shape[0]
    col_width = parent_front.shape[1]
    slab = pivot_span // panel_count
    slabs_per_block = col_width // slab

    panel_all = child_panel[0]
    own_panel = lax.dynamic_slice_in_dim(panel_all, panel_id * child_rows, child_rows, 0)
    update = child_front[0] - lax.dot_general(
        own_panel, panel_all, (((1,), (1,)), ((), ())), preferred_element_type=jnp.float32
    )
    mapped = tile_map[0]
    live_tiles = jnp.arange(tiles_child, dtype=jnp.int32) < tile_count[0]
    everywhere = jnp.arange(tiles_front, dtype=jnp.int32)
    chosen = ((mapped[None, :] == everywhere[:, None]) & live_tiles[None, :]).astype(jnp.float32)
    placed = jnp.einsum(
        "rtb,ft->rfb", update.reshape(child_rows, tiles_child, TILE), chosen, precision=highest
    ).reshape(child_rows, NF)
    regular = placed.reshape(child_rows, panel_count, col_width).transpose(1, 0, 2)
    pivot_slabs = placed[:, :pivot_span].reshape(child_rows, panel_count, slab).transpose(1, 0, 2)
    parent_slabs = parent_front.reshape(height, slabs_per_block, slab).transpose(1, 0, 2)
    parent_slabs = jnp.tile(parent_slabs, (panel_count // slabs_per_block, 1, 1))
    dest = jnp.arange(panel_count, dtype=jnp.int32)
    parent_slabs = jnp.where(
        (dest // slabs_per_block == panel_id)[:, None, None], parent_slabs, 0.0
    )
    send_slabs = jnp.concatenate([pivot_slabs, parent_slabs], axis=2)
    moved_slabs = lax.all_to_all(send_slabs, "panel", split_axis=0, concat_axis=0, tiled=True)
    moved = lax.all_to_all(regular, "panel", split_axis=0, concat_axis=0, tiled=True)
    parent_slab = jnp.sum(moved_slabs[:, :, slab:], axis=0)
    targets = jnp.arange(leaf_count * height // TILE, dtype=jnp.int32)
    picked = ((mapped[None, :] == targets[:, None]) & live_tiles[None, :]).astype(jnp.float32)
    picked = jnp.concatenate([picked, (targets == leaf_id).astype(jnp.float32)[:, None]], axis=1)
    slab_sources = jnp.concatenate([moved_slabs[:, :, :slab], parent_slab[None]], axis=0)
    slab_rows = jnp.einsum("ft,tbc->fbc", picked, slab_sources, precision=highest)
    slab_rows = slab_rows.reshape(leaf_count * height, slab)
    top_share = pivot_span // leaf_count
    slab_rows = jnp.concatenate(
        [
            slab_rows[:pivot_span].reshape(leaf_count, top_share, slab),
            slab_rows[pivot_span:].reshape(leaf_count, height - top_share, slab),
        ],
        axis=1,
    ).reshape(leaf_count * height, slab)
    my_slab = lax.psum_scatter(slab_rows, "leaf", scatter_dimension=0, tiled=True)
    sources = jnp.concatenate([moved, parent_front[None]], axis=0)
    summed = jnp.einsum("ft,tbc->fbc", picked, sources, precision=highest)
    front_block = lax.psum_scatter(
        summed.reshape(leaf_count * height, col_width), "leaf", scatter_dimension=0, tiled=True
    )

    def assemble(piece):
        rows = piece.shape[0]
        got = lax.all_gather(piece, ("leaf", "panel"), axis=0, tiled=False)
        got = got.reshape(leaf_count, panel_count, rows, slab).transpose(0, 2, 1, 3)
        return got.reshape(leaf_count * rows, panel_count * slab)

    pivot_block = assemble(my_slab[:top_share])
    lower_share = height - top_share
    lower_pieces = lax.all_gather(my_slab[top_share:], ("leaf", "panel"), axis=0, tiled=False)
    lower_pieces = lower_pieces.reshape(leaf_count, panel_count, lower_share, slab)

    def lower_rows(first, count):
        span = -(-(count + lower_share - 1) // lower_share)
        start = jnp.minimum(first // lower_share, leaf_count - span)
        pieces = lax.dynamic_slice_in_dim(lower_pieces, start, span, 0)
        pieces = pieces.transpose(0, 2, 1, 3).reshape(span * lower_share, panel_count * slab)
        return lax.dynamic_slice_in_dim(pieces, first - start * lower_share, count, 0)

    blocks = pivot_span // FACTOR_TILE
    eye = jnp.eye(FACTOR_TILE, dtype=jnp.float32)
    work = pivot_block
    factor_cols = []
    inverses = []
    for k in range(blocks):
        lo, hi = k * FACTOR_TILE, (k + 1) * FACTOR_TILE
        diag = lax.linalg.cholesky(work[lo:hi, lo:hi], symmetrize_input=True)
        diag = jnp.tril(diag)
        inverse = lax.linalg.triangular_solve(diag, eye, left_side=True, lower=True)
        inverses.append(inverse)
        if k + 1 < blocks:
            below = jnp.dot(work[hi:, lo:hi], inverse.T, precision=highest)
            work = work.at[hi:, hi:].add(-jnp.dot(below, below.T, precision=highest))
            column = jnp.concatenate([jnp.zeros((lo, FACTOR_TILE), jnp.float32), diag, below], axis=0)
        else:
            column = jnp.concatenate([jnp.zeros((lo, FACTOR_TILE), jnp.float32), diag], axis=0)
        factor_cols.append(column)
    factor = jnp.concatenate(factor_cols, axis=1)

    top_tiles = pivot_span // height
    own_rows = lower_rows(jnp.maximum(leaf_id - top_tiles, 0) * height, height)
    col_rows = lower_rows(jnp.maximum(panel_id - pivot_span // col_width, 0) * col_width, col_width)
    extra = jnp.concatenate([own_rows, col_rows], axis=0)
    solved = []
    for k in range(blocks):
        lo, hi = k * FACTOR_TILE, (k + 1) * FACTOR_TILE
        part = extra[:, lo:hi]
        if k:
            part = part - jnp.dot(
                jnp.concatenate(solved, axis=1), factor[lo:hi, :lo].T, precision=highest
            )
        solved.append(jnp.dot(part, inverses[k].T, precision=highest))
    solved = jnp.concatenate(solved, axis=1)

    factor_rows = lax.dynamic_slice_in_dim(
        factor, jnp.minimum(leaf_id, top_tiles - 1) * height, height, 0
    )
    row_part = jnp.where(leaf_id < top_tiles, factor_rows, solved[:height])
    col_part = solved[height:]
    rest = front_block - lax.dot_general(
        row_part,
        col_part,
        (((1,), (1,)), ((), ())),
        precision=highest,
        preferred_element_type=jnp.float32,
    )
    pivot_blocks = pivot_span // col_width
    pivot_out = lax.dynamic_slice_in_dim(
        row_part, jnp.minimum(panel_id, pivot_blocks - 1) * col_width, col_width, 1
    )
    upper = jnp.where(leaf_id < top_tiles, 0.0, rest)
    return jnp.where(panel_id < pivot_blocks, pivot_out, upper)


def solution(mesh):
    placed = (
        P("leaf", "panel", None),
        P("leaf", None, None),
        P("leaf", "panel"),
        P("leaf", None),
        P("leaf"),
    )
    return jax.shard_map(
        shards, mesh=mesh, in_specs=placed, out_specs=P("leaf", "panel"), check_vma=False
    )
```

```python
import jax
import jax.numpy as jnp
from jax import lax
from jax.sharding import PartitionSpec as P

TILE = 256
NF = 4096
CB = 2048
STEPS = 4
FACTOR_TILE = 128


def shards(child_front, child_panel, parent_front, tile_map, tile_count):
    highest = lax.Precision.HIGHEST
    panel_count = lax.axis_size("panel")
    leaf_count = lax.axis_size("leaf")
    leaf_id = lax.axis_index("leaf")
    panel_id = lax.axis_index("panel")
    tiles_child = CB // TILE
    tiles_front = NF // TILE
    pivot_span = STEPS * TILE
    child_rows = child_front.shape[1]
    height = parent_front.shape[0]
    col_width = parent_front.shape[1]
    slab = pivot_span // panel_count
    slabs_per_block = col_width // slab

    panel_all = child_panel[0]
    own_panel = lax.dynamic_slice_in_dim(panel_all, panel_id * child_rows, child_rows, 0)
    update = child_front[0] - lax.dot_general(
        own_panel, panel_all, (((1,), (1,)), ((), ())), preferred_element_type=jnp.float32
    )
    mapped = tile_map[0]
    live_tiles = jnp.arange(tiles_child, dtype=jnp.int32) < tile_count[0]
    everywhere = jnp.arange(tiles_front, dtype=jnp.int32)
    chosen = ((mapped[None, :] == everywhere[:, None]) & live_tiles[None, :]).astype(jnp.float32)
    placed = jnp.einsum(
        "rtb,ft->rfb", update.reshape(child_rows, tiles_child, TILE), chosen, precision=highest
    ).reshape(child_rows, NF)
    regular = placed.reshape(child_rows, panel_count, col_width).transpose(1, 0, 2)
    pivot_slabs = placed[:, :pivot_span].reshape(child_rows, panel_count, slab).transpose(1, 0, 2)
    parent_slabs = parent_front.reshape(height, slabs_per_block, slab).transpose(1, 0, 2)
    parent_slabs = jnp.tile(parent_slabs, (panel_count // slabs_per_block, 1, 1))
    dest = jnp.arange(panel_count, dtype=jnp.int32)
    parent_slabs = jnp.where(
        (dest // slabs_per_block == panel_id)[:, None, None], parent_slabs, 0.0
    )
    send_slabs = jnp.concatenate([pivot_slabs, parent_slabs], axis=2)
    moved_slabs = lax.all_to_all(send_slabs, "panel", split_axis=0, concat_axis=0, tiled=True)
    moved = lax.all_to_all(regular, "panel", split_axis=0, concat_axis=0, tiled=True)
    parent_slab = jnp.sum(moved_slabs[:, :, slab:], axis=0)
    targets = jnp.arange(leaf_count * height // TILE, dtype=jnp.int32)
    picked = ((mapped[None, :] == targets[:, None]) & live_tiles[None, :]).astype(jnp.float32)
    picked = jnp.concatenate([picked, (targets == leaf_id).astype(jnp.float32)[:, None]], axis=1)
    slab_sources = jnp.concatenate([moved_slabs[:, :, :slab], parent_slab[None]], axis=0)
    slab_rows = jnp.einsum("ft,tbc->fbc", picked, slab_sources, precision=highest)
    slab_rows = slab_rows.reshape(leaf_count * height, slab)
    my_slab = lax.psum_scatter(slab_rows, "leaf", scatter_dimension=0, tiled=True)
    sources = jnp.concatenate([moved, parent_front[None]], axis=0)
    summed = jnp.einsum("ft,tbc->fbc", picked, sources, precision=highest)
    front_block = lax.psum_scatter(
        summed.reshape(leaf_count * height, col_width), "leaf", scatter_dimension=0, tiled=True
    )

    gathered = lax.all_gather(my_slab, ("leaf", "panel"), axis=0, tiled=False)
    gathered = gathered.reshape(leaf_count, panel_count, height, slab)

    def rows_of(tiles):
        count = tiles.shape[0]
        return tiles.transpose(0, 2, 1, 3).reshape(count * height, panel_count * slab)

    top_tiles = pivot_span // height
    col_tiles = col_width // height
    own_rows = rows_of(lax.dynamic_slice_in_dim(gathered, leaf_id, 1, 0))
    col_rows = rows_of(lax.dynamic_slice_in_dim(gathered, panel_id * col_tiles, col_tiles, 0))
    work = jnp.concatenate([rows_of(gathered[:top_tiles]), own_rows, col_rows], axis=0)

    blocks = pivot_span // FACTOR_TILE
    eye = jnp.eye(FACTOR_TILE, dtype=jnp.float32)
    factor_cols = []
    solved = []
    for k in range(blocks):
        lo, hi = k * FACTOR_TILE, (k + 1) * FACTOR_TILE
        diag = lax.linalg.cholesky(work[lo:hi, lo:hi], symmetrize_input=True)
        diag = jnp.tril(diag)
        inverse = lax.linalg.triangular_solve(diag, eye, left_side=True, lower=True)
        below = jnp.dot(work[hi:, lo:hi], inverse.T, precision=highest)
        if hi < pivot_span:
            work = work.at[hi:, hi:].add(
                -jnp.dot(below, below[: pivot_span - hi].T, precision=highest)
            )
        factor_cols.append(
            jnp.concatenate(
                [jnp.zeros((lo, FACTOR_TILE), jnp.float32), diag, below[: pivot_span - hi]], axis=0
            )
        )
        solved.append(below[pivot_span - hi :])
    factor = jnp.concatenate(factor_cols, axis=1)
    solved = jnp.concatenate(solved, axis=1)

    factor_rows = lax.dynamic_slice_in_dim(
        factor, jnp.minimum(leaf_id, top_tiles - 1) * height, height, 0
    )
    row_part = jnp.where(leaf_id < top_tiles, factor_rows, solved[:height])
    col_part = solved[height:]
    rest = front_block - lax.dot_general(
        row_part,
        col_part,
        (((1,), (1,)), ((), ())),
        precision=highest,
        preferred_element_type=jnp.float32,
    )
    pivot_blocks = pivot_span // col_width
    pivot_out = lax.dynamic_slice_in_dim(
        row_part, jnp.minimum(panel_id, pivot_blocks - 1) * col_width, col_width, 1
    )
    upper = jnp.where(leaf_id < top_tiles, 0.0, rest)
    return jnp.where(panel_id < pivot_blocks, pivot_out, upper)


def solution(mesh):
    placed = (
        P("leaf", "panel", None),
        P("leaf", None, None),
        P("leaf", "panel"),
        P("leaf", None),
        P("leaf"),
    )
    return jax.shard_map(
        shards, mesh=mesh, in_specs=placed, out_specs=P("leaf", "panel"), check_vma=False
    )
```

```python
import jax
import jax.numpy as jnp
from jax import lax
from jax.sharding import PartitionSpec as P

TILE = 256
NF = 4096
CB = 2048
STEPS = 4
FACTOR_TILE = 128


def shards(child_front, child_panel, parent_front, tile_map, tile_count):
    highest = lax.Precision.HIGHEST
    high = lax.Precision.HIGH
    panel_count = lax.axis_size("panel")
    leaf_count = lax.axis_size("leaf")
    leaf_id = lax.axis_index("leaf")
    panel_id = lax.axis_index("panel")
    tiles_child = CB // TILE
    tiles_front = NF // TILE
    pivot_span = STEPS * TILE
    child_rows = child_front.shape[1]
    height = parent_front.shape[0]
    col_width = parent_front.shape[1]
    slab = pivot_span // panel_count
    slabs_per_block = col_width // slab

    panel_all = child_panel[0]
    own_panel = lax.dynamic_slice_in_dim(panel_all, panel_id * child_rows, child_rows, 0)
    update = child_front[0] - lax.dot_general(
        own_panel, panel_all, (((1,), (1,)), ((), ())), preferred_element_type=jnp.float32
    )
    mapped = tile_map[0]
    live_tiles = jnp.arange(tiles_child, dtype=jnp.int32) < tile_count[0]
    everywhere = jnp.arange(tiles_front, dtype=jnp.int32)
    chosen = ((mapped[None, :] == everywhere[:, None]) & live_tiles[None, :]).astype(jnp.float32)
    placed = jnp.einsum(
        "rtb,ft->rfb", update.reshape(child_rows, tiles_child, TILE), chosen, precision=highest
    ).reshape(child_rows, NF)
    regular = placed.reshape(child_rows, panel_count, col_width).transpose(1, 0, 2)
    pivot_slabs = placed[:, :pivot_span].reshape(child_rows, panel_count, slab).transpose(1, 0, 2)
    parent_slabs = parent_front.reshape(height, slabs_per_block, slab).transpose(1, 0, 2)
    parent_slabs = jnp.tile(parent_slabs, (panel_count // slabs_per_block, 1, 1))
    dest = jnp.arange(panel_count, dtype=jnp.int32)
    parent_slabs = jnp.where(
        (dest // slabs_per_block == panel_id)[:, None, None], parent_slabs, 0.0
    )
    send_slabs = jnp.concatenate([pivot_slabs, parent_slabs], axis=2)
    moved_slabs = lax.all_to_all(send_slabs, "panel", split_axis=0, concat_axis=0, tiled=True)
    moved = lax.all_to_all(regular, "panel", split_axis=0, concat_axis=0, tiled=True)
    parent_slab = jnp.sum(moved_slabs[:, :, slab:], axis=0)
    targets = jnp.arange(leaf_count * height // TILE, dtype=jnp.int32)
    picked = ((mapped[None, :] == targets[:, None]) & live_tiles[None, :]).astype(jnp.float32)
    picked = jnp.concatenate([picked, (targets == leaf_id).astype(jnp.float32)[:, None]], axis=1)
    slab_sources = jnp.concatenate([moved_slabs[:, :, :slab], parent_slab[None]], axis=0)
    slab_rows = jnp.einsum("ft,tbc->fbc", picked, slab_sources, precision=highest)
    slab_rows = slab_rows.reshape(leaf_count * height, slab)
    my_slab = lax.psum_scatter(slab_rows, "leaf", scatter_dimension=0, tiled=True)
    sources = jnp.concatenate([moved, parent_front[None]], axis=0)
    summed = jnp.einsum("ft,tbc->fbc", picked, sources, precision=highest)
    front_block = lax.psum_scatter(
        summed.reshape(leaf_count * height, col_width), "leaf", scatter_dimension=0, tiled=True
    )

    gathered = lax.all_gather(my_slab, ("leaf", "panel"), axis=0, tiled=False)
    gathered = gathered.reshape(leaf_count, panel_count, height, slab)

    def rows_of(tiles):
        count = tiles.shape[0]
        return tiles.transpose(0, 2, 1, 3).reshape(count * height, panel_count * slab)

    top_tiles = pivot_span // height
    col_tiles = col_width // height
    own_rows = rows_of(lax.dynamic_slice_in_dim(gathered, leaf_id, 1, 0))
    col_rows = rows_of(lax.dynamic_slice_in_dim(gathered, panel_id * col_tiles, col_tiles, 0))
    work = jnp.concatenate([rows_of(gathered[:top_tiles]), own_rows, col_rows], axis=0)

    blocks = pivot_span // FACTOR_TILE
    eye = jnp.eye(FACTOR_TILE, dtype=jnp.float32)
    factor_cols = []
    solved = []
    for k in range(blocks):
        lo, hi = k * FACTOR_TILE, (k + 1) * FACTOR_TILE
        diag = lax.linalg.cholesky(work[lo:hi, lo:hi], symmetrize_input=True)
        diag = jnp.tril(diag)
        inverse = lax.linalg.triangular_solve(diag, eye, left_side=True, lower=True)
        below = jnp.dot(work[hi:, lo:hi], inverse.T, precision=high)
        if hi < pivot_span:
            work = work.at[hi:, hi:].add(
                -jnp.dot(below, below[: pivot_span - hi].T, precision=high)
            )
        factor_cols.append(
            jnp.concatenate(
                [jnp.zeros((lo, FACTOR_TILE), jnp.float32), diag, below[: pivot_span - hi]], axis=0
            )
        )
        solved.append(below[pivot_span - hi :])
    factor = jnp.concatenate(factor_cols, axis=1)
    solved = jnp.concatenate(solved, axis=1)

    factor_rows = lax.dynamic_slice_in_dim(
        factor, jnp.minimum(leaf_id, top_tiles - 1) * height, height, 0
    )
    row_part = jnp.where(leaf_id < top_tiles, factor_rows, solved[:height])
    col_part = solved[height:]
    rest = front_block - lax.dot_general(
        row_part,
        col_part,
        (((1,), (1,)), ((), ())),
        precision=high,
        preferred_element_type=jnp.float32,
    )
    pivot_blocks = pivot_span // col_width
    pivot_out = lax.dynamic_slice_in_dim(
        row_part, jnp.minimum(panel_id, pivot_blocks - 1) * col_width, col_width, 1
    )
    upper = jnp.where(leaf_id < top_tiles, 0.0, rest)
    return jnp.where(panel_id < pivot_blocks, pivot_out, upper)


def solution(mesh):
    placed = (
        P("leaf", "panel", None),
        P("leaf", None, None),
        P("leaf", "panel"),
        P("leaf", None),
        P("leaf"),
    )
    return jax.shard_map(
        shards, mesh=mesh, in_specs=placed, out_specs=P("leaf", "panel"), check_vma=False
    )
```

```python
import jax
import jax.numpy as jnp
from jax import lax
from jax.sharding import PartitionSpec as P

TILE = 256
NF = 4096
CB = 2048
STEPS = 4
FACTOR_TILE = 128


def shards_body(child_front, child_panel, parent_front, tile_map, tile_count):
    highest = lax.Precision.HIGHEST
    high = lax.Precision.HIGH
    panel_count = lax.axis_size("panel")
    leaf_count = lax.axis_size("leaf")
    leaf_id = lax.axis_index("leaf")
    panel_id = lax.axis_index("panel")
    tiles_child = CB // TILE
    tiles_front = NF // TILE
    pivot_span = STEPS * TILE
    child_rows = child_front.shape[1]
    height = parent_front.shape[0]
    col_width = parent_front.shape[1]
    slab = pivot_span // panel_count
    slabs_per_block = col_width // slab

    panel_all = child_panel[0]
    own_panel = lax.dynamic_slice_in_dim(panel_all, panel_id * child_rows, child_rows, 0)
    mapped = tile_map[0]
    live_tiles = jnp.arange(tiles_child, dtype=jnp.int32) < tile_count[0]
    everywhere = jnp.arange(tiles_front, dtype=jnp.int32)
    chosen = ((mapped[None, :] == everywhere[:, None]) & live_tiles[None, :]).astype(jnp.float32)
    lead = min(pivot_span, CB)
    lead_tiles = lead // TILE
    pivot_tiles = pivot_span // TILE

    def child_update(first, count):
        return child_front[0][:, first : first + count] - lax.dot_general(
            own_panel,
            panel_all[first : first + count],
            (((1,), (1,)), ((), ())),
            preferred_element_type=jnp.float32,
        )

    update_lead = child_update(0, lead)
    placed_pivot = jnp.einsum(
        "rtb,ft->rfb",
        update_lead.reshape(child_rows, lead_tiles, TILE),
        chosen[:pivot_tiles, :lead_tiles],
        precision=highest,
    ).reshape(child_rows, pivot_span)
    update = jnp.concatenate([update_lead, child_update(lead, CB - lead)], axis=1)
    placed = jnp.einsum(
        "rtb,ft->rfb", update.reshape(child_rows, tiles_child, TILE), chosen, precision=highest
    ).reshape(child_rows, NF)
    regular = placed.reshape(child_rows, panel_count, col_width).transpose(1, 0, 2)
    pivot_slabs = placed_pivot.reshape(child_rows, panel_count, slab).transpose(1, 0, 2)
    parent_slabs = parent_front.reshape(height, slabs_per_block, slab).transpose(1, 0, 2)
    parent_slabs = jnp.tile(parent_slabs, (panel_count // slabs_per_block, 1, 1))
    dest = jnp.arange(panel_count, dtype=jnp.int32)
    parent_slabs = jnp.where(
        (dest // slabs_per_block == panel_id)[:, None, None], parent_slabs, 0.0
    )
    send_slabs = jnp.concatenate([pivot_slabs, parent_slabs], axis=2)
    moved_slabs = lax.all_to_all(send_slabs, "panel", split_axis=0, concat_axis=0, tiled=True)
    moved = lax.all_to_all(regular, "panel", split_axis=0, concat_axis=0, tiled=True)
    parent_slab = jnp.sum(moved_slabs[:, :, slab:], axis=0)
    targets = jnp.arange(leaf_count * height // TILE, dtype=jnp.int32)
    picked = ((mapped[None, :] == targets[:, None]) & live_tiles[None, :]).astype(jnp.float32)
    picked = jnp.concatenate([picked, (targets == leaf_id).astype(jnp.float32)[:, None]], axis=1)
    slab_sources = jnp.concatenate([moved_slabs[:, :, :slab], parent_slab[None]], axis=0)
    slab_rows = jnp.einsum("ft,tbc->fbc", picked, slab_sources, precision=highest)
    slab_rows = slab_rows.reshape(leaf_count * height, slab)
    my_slab = lax.psum_scatter(slab_rows, "leaf", scatter_dimension=0, tiled=True)
    sources = jnp.concatenate([moved, parent_front[None]], axis=0)
    summed = jnp.einsum("ft,tbc->fbc", picked, sources, precision=highest)
    front_block = lax.psum_scatter(
        summed.reshape(leaf_count * height, col_width), "leaf", scatter_dimension=0, tiled=True
    )

    gathered = lax.all_gather(my_slab, ("leaf", "panel"), axis=0, tiled=False)
    gathered = gathered.reshape(leaf_count, panel_count, height, slab)

    def rows_of(tiles):
        count = tiles.shape[0]
        return tiles.transpose(0, 2, 1, 3).reshape(count * height, panel_count * slab)

    top_tiles = pivot_span // height
    col_tiles = col_width // height
    own_rows = rows_of(lax.dynamic_slice_in_dim(gathered, leaf_id, 1, 0))
    col_rows = rows_of(lax.dynamic_slice_in_dim(gathered, panel_id * col_tiles, col_tiles, 0))
    work = jnp.concatenate([rows_of(gathered[:top_tiles]), own_rows, col_rows], axis=0)

    blocks = pivot_span // FACTOR_TILE
    eye = jnp.eye(FACTOR_TILE, dtype=jnp.float32)
    factor_cols = []
    solved = []
    for k in range(blocks):
        lo, hi = k * FACTOR_TILE, (k + 1) * FACTOR_TILE
        diag = lax.linalg.cholesky(work[lo:hi, lo:hi], symmetrize_input=False)
        diag = jnp.tril(diag)
        inverse = lax.linalg.triangular_solve(diag, eye, left_side=True, lower=True)
        below = jnp.dot(work[hi:, lo:hi], inverse.T, precision=high)
        if hi < pivot_span:
            work = work.at[hi:, hi:].add(
                -jnp.dot(below, below[: pivot_span - hi].T, precision=high)
            )
        factor_cols.append(
            jnp.concatenate(
                [jnp.zeros((lo, FACTOR_TILE), jnp.float32), diag, below[: pivot_span - hi]], axis=0
            )
        )
        solved.append(below[pivot_span - hi :])
    factor = jnp.concatenate(factor_cols, axis=1)
    solved = jnp.concatenate(solved, axis=1)

    factor_rows = lax.dynamic_slice_in_dim(
        factor, jnp.minimum(leaf_id, top_tiles - 1) * height, height, 0
    )
    row_part = jnp.where(leaf_id < top_tiles, factor_rows, solved[:height])
    col_part = solved[height:]
    rest = front_block - lax.dot_general(
        row_part,
        col_part,
        (((1,), (1,)), ((), ())),
        precision=high,
        preferred_element_type=jnp.float32,
    )
    pivot_blocks = pivot_span // col_width
    pivot_out = lax.dynamic_slice_in_dim(
        row_part, jnp.minimum(panel_id, pivot_blocks - 1) * col_width, col_width, 1
    )
    upper = jnp.where(leaf_id < top_tiles, 0.0, rest)
    return jnp.where(panel_id < pivot_blocks, pivot_out, upper)


def solution(mesh):
    placed = (
        P("leaf", "panel", None),
        P("leaf", None, None),
        P("leaf", "panel"),
        P("leaf", None),
        P("leaf"),
    )
    return jax.shard_map(
        shards_body, mesh=mesh, in_specs=placed, out_specs=P("leaf", "panel"), check_vma=False
    )
```

```python
import jax
import jax.numpy as jnp
from jax import lax
from jax.sharding import PartitionSpec as P

TILE = 256
NF = 4096
CB = 2048
STEPS = 4
FACTOR_TILE = 128


def shards_body(child_front, child_panel, parent_front, tile_map, tile_count):
    highest = lax.Precision.HIGHEST
    high = lax.Precision.HIGH
    panel_count = lax.axis_size("panel")
    leaf_count = lax.axis_size("leaf")
    leaf_id = lax.axis_index("leaf")
    panel_id = lax.axis_index("panel")
    tiles_child = CB // TILE
    tiles_front = NF // TILE
    pivot_span = STEPS * TILE
    child_rows = child_front.shape[1]
    height = parent_front.shape[0]
    col_width = parent_front.shape[1]
    slab = pivot_span // panel_count
    slabs_per_block = col_width // slab

    panel_all = child_panel[0]
    own_panel = lax.dynamic_slice_in_dim(panel_all, panel_id * child_rows, child_rows, 0)
    mapped = tile_map[0]
    live_tiles = jnp.arange(tiles_child, dtype=jnp.int32) < tile_count[0]
    everywhere = jnp.arange(tiles_front, dtype=jnp.int32)
    chosen = ((mapped[None, :] == everywhere[:, None]) & live_tiles[None, :]).astype(jnp.float32)
    lead = min(pivot_span, CB)
    lead_tiles = lead // TILE
    pivot_tiles = pivot_span // TILE

    def child_update(first, count):
        return child_front[0][:, first : first + count] - lax.dot_general(
            own_panel,
            panel_all[first : first + count],
            (((1,), (1,)), ((), ())),
            preferred_element_type=jnp.float32,
        )

    update_lead = child_update(0, lead)
    placed_pivot = jnp.einsum(
        "rtb,ft->rfb",
        update_lead.reshape(child_rows, lead_tiles, TILE),
        chosen[:pivot_tiles, :lead_tiles],
        precision=highest,
    ).reshape(child_rows, pivot_span)
    update = jnp.concatenate([update_lead, child_update(lead, CB - lead)], axis=1)
    placed = jnp.einsum(
        "rtb,ft->rfb", update.reshape(child_rows, tiles_child, TILE), chosen, precision=highest
    ).reshape(child_rows, NF)
    regular = placed.reshape(child_rows, panel_count, col_width).transpose(1, 0, 2)
    pivot_slabs = placed_pivot.reshape(child_rows, panel_count, slab).transpose(1, 0, 2)
    parent_slabs = parent_front.reshape(height, slabs_per_block, slab).transpose(1, 0, 2)
    parent_slabs = jnp.tile(parent_slabs, (panel_count // slabs_per_block, 1, 1))
    dest = jnp.arange(panel_count, dtype=jnp.int32)
    parent_slabs = jnp.where(
        (dest // slabs_per_block == panel_id)[:, None, None], parent_slabs, 0.0
    )
    send_slabs = jnp.concatenate([pivot_slabs, parent_slabs], axis=2)
    both = lax.all_to_all(
        jnp.concatenate([send_slabs, regular], axis=2), "panel", split_axis=0, concat_axis=0, tiled=True
    )
    moved_slabs = both[:, :, : 2 * slab]
    moved = both[:, :, 2 * slab :]
    parent_slab = jnp.sum(moved_slabs[:, :, slab:], axis=0)
    targets = jnp.arange(leaf_count * height // TILE, dtype=jnp.int32)
    picked = ((mapped[None, :] == targets[:, None]) & live_tiles[None, :]).astype(jnp.float32)
    picked = jnp.concatenate([picked, (targets == leaf_id).astype(jnp.float32)[:, None]], axis=1)
    slab_sources = jnp.concatenate([moved_slabs[:, :, :slab], parent_slab[None]], axis=0)
    slab_rows = jnp.einsum("ft,tbc->fbc", picked, slab_sources, precision=highest)
    slab_rows = slab_rows.reshape(leaf_count * height, slab)
    pieces = lax.all_to_all(
        slab_rows.reshape(leaf_count, height, slab), "leaf", split_axis=0, concat_axis=0, tiled=True
    )
    my_slab = jnp.sum(pieces, axis=0)
    sources = jnp.concatenate([moved, parent_front[None]], axis=0)
    summed = jnp.einsum("ft,tbc->fbc", picked, sources, precision=highest)
    front_block = lax.psum_scatter(
        summed.reshape(leaf_count * height, col_width), "leaf", scatter_dimension=0, tiled=True
    )

    gathered = lax.all_gather(my_slab, ("leaf", "panel"), axis=0, tiled=False)
    gathered = gathered.reshape(leaf_count, panel_count, height, slab)

    def rows_of(tiles):
        count = tiles.shape[0]
        return tiles.transpose(0, 2, 1, 3).reshape(count * height, panel_count * slab)

    top_tiles = pivot_span // height
    col_tiles = col_width // height
    own_rows = rows_of(lax.dynamic_slice_in_dim(gathered, leaf_id, 1, 0))
    col_rows = rows_of(lax.dynamic_slice_in_dim(gathered, panel_id * col_tiles, col_tiles, 0))
    work = jnp.concatenate([rows_of(gathered[:top_tiles]), own_rows, col_rows], axis=0)

    blocks = pivot_span // FACTOR_TILE
    eye = jnp.eye(FACTOR_TILE, dtype=jnp.float32)
    factor_cols = []
    solved = []
    for k in range(blocks):
        lo, hi = k * FACTOR_TILE, (k + 1) * FACTOR_TILE
        diag = lax.linalg.cholesky(work[lo:hi, lo:hi], symmetrize_input=False)
        diag = jnp.tril(diag)
        inverse = lax.linalg.triangular_solve(diag, eye, left_side=True, lower=True)
        below = jnp.dot(work[hi:, lo:hi], inverse.T, precision=high)
        if hi < pivot_span:
            work = work.at[hi:, hi:].add(
                -jnp.dot(below, below[: pivot_span - hi].T, precision=high)
            )
        factor_cols.append(
            jnp.concatenate(
                [jnp.zeros((lo, FACTOR_TILE), jnp.float32), diag, below[: pivot_span - hi]], axis=0
            )
        )
        solved.append(below[pivot_span - hi :])
    factor = jnp.concatenate(factor_cols, axis=1)
    solved = jnp.concatenate(solved, axis=1)

    factor_rows = lax.dynamic_slice_in_dim(
        factor, jnp.minimum(leaf_id, top_tiles - 1) * height, height, 0
    )
    row_part = jnp.where(leaf_id < top_tiles, factor_rows, solved[:height])
    col_part = solved[height:]
    rest = front_block - lax.dot_general(
        row_part,
        col_part,
        (((1,), (1,)), ((), ())),
        precision=high,
        preferred_element_type=jnp.float32,
    )
    pivot_blocks = pivot_span // col_width
    pivot_out = lax.dynamic_slice_in_dim(
        row_part, jnp.minimum(panel_id, pivot_blocks - 1) * col_width, col_width, 1
    )
    upper = jnp.where(leaf_id < top_tiles, 0.0, rest)
    return jnp.where(panel_id < pivot_blocks, pivot_out, upper)


def solution(mesh):
    placed = (
        P("leaf", "panel", None),
        P("leaf", None, None),
        P("leaf", "panel"),
        P("leaf", None),
        P("leaf"),
    )
    return jax.shard_map(
        shards_body, mesh=mesh, in_specs=placed, out_specs=P("leaf", "panel"), check_vma=False
    )
```

```python
import jax
import jax.numpy as jnp
from jax import lax
from jax.sharding import PartitionSpec as P

TILE = 256
NF = 4096
CB = 2048
STEPS = 4
FACTOR_TILE = 128


def shards_body(child_front, child_panel, parent_front, tile_map, tile_count):
    highest = lax.Precision.HIGHEST
    high = lax.Precision.HIGH
    panel_count = lax.axis_size("panel")
    leaf_count = lax.axis_size("leaf")
    leaf_id = lax.axis_index("leaf")
    panel_id = lax.axis_index("panel")
    tiles_child = CB // TILE
    tiles_front = NF // TILE
    pivot_span = STEPS * TILE
    child_rows = child_front.shape[1]
    height = parent_front.shape[0]
    col_width = parent_front.shape[1]
    slab = pivot_span // panel_count
    slabs_per_block = col_width // slab

    panel_all = child_panel[0]
    own_panel = lax.dynamic_slice_in_dim(panel_all, panel_id * child_rows, child_rows, 0)
    mapped = tile_map[0]
    live_tiles = jnp.arange(tiles_child, dtype=jnp.int32) < tile_count[0]
    everywhere = jnp.arange(tiles_front, dtype=jnp.int32)
    chosen = ((mapped[None, :] == everywhere[:, None]) & live_tiles[None, :]).astype(jnp.float32)
    lead = min(pivot_span, CB)
    lead_tiles = lead // TILE
    pivot_tiles = pivot_span // TILE

    def child_update(first, count):
        return child_front[0][:, first : first + count] - lax.dot_general(
            own_panel,
            panel_all[first : first + count],
            (((1,), (1,)), ((), ())),
            preferred_element_type=jnp.float32,
        )

    update_lead = child_update(0, lead)
    placed_pivot = jnp.einsum(
        "rtb,ft->rfb",
        update_lead.reshape(child_rows, lead_tiles, TILE),
        chosen[:pivot_tiles, :lead_tiles],
        precision=highest,
    ).reshape(child_rows, pivot_span)
    update = jnp.concatenate([update_lead, child_update(lead, CB - lead)], axis=1)
    placed = jnp.einsum(
        "rtb,ft->rfb", update.reshape(child_rows, tiles_child, TILE), chosen, precision=highest
    ).reshape(child_rows, NF)
    regular = placed.reshape(child_rows, panel_count, col_width).transpose(1, 0, 2)
    pivot_slabs = placed_pivot.reshape(child_rows, panel_count, slab).transpose(1, 0, 2)
    parent_slabs = parent_front.reshape(height, slabs_per_block, slab).transpose(1, 0, 2)
    parent_slabs = jnp.tile(parent_slabs, (panel_count // slabs_per_block, 1, 1))
    dest = jnp.arange(panel_count, dtype=jnp.int32)
    parent_slabs = jnp.where(
        (dest // slabs_per_block == panel_id)[:, None, None], parent_slabs, 0.0
    )
    send_slabs = jnp.concatenate([pivot_slabs, parent_slabs], axis=2)
    moved_slabs = lax.all_to_all(send_slabs, "panel", split_axis=0, concat_axis=0, tiled=True)
    moved = lax.all_to_all(regular, "panel", split_axis=0, concat_axis=0, tiled=True)
    parent_slab = jnp.sum(moved_slabs[:, :, slab:], axis=0)
    targets = jnp.arange(leaf_count * height // TILE, dtype=jnp.int32)
    picked = ((mapped[None, :] == targets[:, None]) & live_tiles[None, :]).astype(jnp.float32)
    picked = jnp.concatenate([picked, (targets == leaf_id).astype(jnp.float32)[:, None]], axis=1)
    slab_sources = jnp.concatenate([moved_slabs[:, :, :slab], parent_slab[None]], axis=0)
    slab_rows = jnp.einsum("ft,tbc->fbc", picked, slab_sources, precision=highest)
    slab_rows = slab_rows.reshape(leaf_count * height, slab)
    slab_rows = slab_rows + 0.0 * regular[0, 0, 0]
    pieces = lax.all_to_all(
        slab_rows.reshape(leaf_count, height, slab), "leaf", split_axis=0, concat_axis=0, tiled=True
    )
    my_slab = jnp.sum(pieces, axis=0)
    sources = jnp.concatenate([moved, parent_front[None]], axis=0)
    summed = jnp.einsum("ft,tbc->fbc", picked, sources, precision=highest)
    front_block = lax.psum_scatter(
        summed.reshape(leaf_count * height, col_width), "leaf", scatter_dimension=0, tiled=True
    )

    gathered = lax.all_gather(my_slab, ("leaf", "panel"), axis=0, tiled=False)
    gathered = gathered.reshape(leaf_count, panel_count, height, slab)

    def rows_of(tiles):
        count = tiles.shape[0]
        return tiles.transpose(0, 2, 1, 3).reshape(count * height, panel_count * slab)

    top_tiles = pivot_span // height
    col_tiles = col_width // height
    own_rows = rows_of(lax.dynamic_slice_in_dim(gathered, leaf_id, 1, 0))
    col_rows = rows_of(lax.dynamic_slice_in_dim(gathered, panel_id * col_tiles, col_tiles, 0))
    work = jnp.concatenate([rows_of(gathered[:top_tiles]), own_rows, col_rows], axis=0)

    blocks = pivot_span // FACTOR_TILE
    eye = jnp.eye(FACTOR_TILE, dtype=jnp.float32)
    factor_cols = []
    solved = []
    for k in range(blocks):
        lo, hi = k * FACTOR_TILE, (k + 1) * FACTOR_TILE
        diag = lax.linalg.cholesky(work[lo:hi, lo:hi], symmetrize_input=False)
        inverse = lax.linalg.triangular_solve(diag, eye, left_side=True, lower=True)
        below = jnp.dot(work[hi:, lo:hi], inverse.T, precision=high)
        if hi < pivot_span:
            work = work.at[hi:, hi:].add(
                -jnp.dot(below, below[: pivot_span - hi].T, precision=high)
            )
        factor_cols.append(
            jnp.concatenate(
                [jnp.zeros((lo, FACTOR_TILE), jnp.float32), diag, below[: pivot_span - hi]], axis=0
            )
        )
        solved.append(below[pivot_span - hi :])
    factor = jnp.tril(jnp.concatenate(factor_cols, axis=1))
    solved = jnp.concatenate(solved, axis=1)

    factor_rows = lax.dynamic_slice_in_dim(
        factor, jnp.minimum(leaf_id, top_tiles - 1) * height, height, 0
    )
    row_part = jnp.where(leaf_id < top_tiles, factor_rows, solved[:height])
    col_part = solved[height:]
    rest = front_block - lax.dot_general(
        row_part,
        col_part,
        (((1,), (1,)), ((), ())),
        precision=high,
        preferred_element_type=jnp.float32,
    )
    pivot_blocks = pivot_span // col_width
    pivot_out = lax.dynamic_slice_in_dim(
        row_part, jnp.minimum(panel_id, pivot_blocks - 1) * col_width, col_width, 1
    )
    upper = jnp.where(leaf_id < top_tiles, 0.0, rest)
    return jnp.where(panel_id < pivot_blocks, pivot_out, upper)


def solution(mesh):
    placed = (
        P("leaf", "panel", None),
        P("leaf", None, None),
        P("leaf", "panel"),
        P("leaf", None),
        P("leaf"),
    )
    return jax.shard_map(
        shards_body, mesh=mesh, in_specs=placed, out_specs=P("leaf", "panel"), check_vma=False
    )
```
